32 devices in a mesh: dp: 4 (over z), ctx: 2 (over y), seq: 4 (over x, core).
Axes of the slice: x: 2, y: 2, z: 4, core: 2. Of those that a mesh axis runs over, the one named last changes fastest.
Arguments:
- layer_input: bfloat16 [16, 1024, 768], P('dp', ('ctx', 'seq')), may hold values from -6 to 6
- block_order: int32 [16, 8], P('dp'), may hold values from 0 to 7, each once within a row
- attn_gain: bfloat16 [768], P(('dp', 'ctx')), may hold values from 0.3984375 to 1.59375
- attn_shift: bfloat16 [768], P(('dp', 'ctx')), may hold values from -3 to 3
- w_qkv: bfloat16 [768, 2304], P(('dp', 'ctx')), may hold values from -0.21875 to 0.21875
- bias_query: bfloat16 [768], P(('dp', 'ctx')), may hold values from -3 to 3
- bias_value: bfloat16 [768], P(('dp', 'ctx')), may hold values from -3 to 3
- w_out: bfloat16 [768, 768], P(('dp', 'ctx')), may hold values from -3 to 3
- bias_out: bfloat16 [768], P(('dp', 'ctx')), may hold values from -3 to 3
- mlp_gain: bfloat16 [768], P(('dp', 'ctx')), may hold values from 0.3984375 to 1.59375
- mlp_shift: bfloat16 [768], P(('dp', 'ctx')), may hold values from -3 to 3
- w_up: bfloat16 [768, 3072], P(('dp', 'ctx')), may hold values from -0.21875 to 0.21875
- bias_up: bfloat16 [3072], P(('dp', 'ctx')), may hold values from -3 to 3
- w_down: bfloat16 [3072, 768], P(('dp', 'ctx')), may hold values from -0.109375 to 0.109375
- bias_down: bfloat16 [768], P(('dp', 'ctx')), may hold values from -3 to 3
- cotangent: bfloat16 [16, 1024, 768], P('dp', ('ctx', 'seq')), may hold values from -6 to 6
Outputs:
- layer_output: bfloat16 [16, 1024, 768], P('dp', ('ctx', 'seq'))
- grad_input: bfloat16 [16, 1024, 768], P('dp', ('ctx', 'seq'))
- grad_attn_gain: float32 [768], P(('dp', 'ctx'))
- grad_attn_shift: float32 [768], P(('dp', 'ctx'))
- grad_w_qkv: float32 [768, 2304], P(('dp', 'ctx'))
- grad_bias_query: float32 [768], P(('dp', 'ctx'))
- grad_bias_value: float32 [768], P(('dp', 'ctx'))
- grad_w_out: float32 [768, 768], P(('dp', 'ctx'))
- grad_bias_out: float32 [768], P(('dp', 'ctx'))
- grad_mlp_gain: float32 [768], P(('dp', 'ctx'))
- grad_mlp_shift: float32 [768], P(('dp', 'ctx'))
- grad_w_up: float32 [768, 3072], P(('dp', 'ctx'))
- grad_bias_up: float32 [3072], P(('dp', 'ctx'))
- grad_w_down: float32 [3072, 768], P(('dp', 'ctx'))
- grad_bias_down: float32 [768], P(('dp', 'ctx'))
The draws below stay inside these ranges and needn't reach their ends.
Inputs may be any that keep to these rules, and one draw needn't show every extreme that they name: Each row of block_order names every block number 0 to 7 once.
All inputs are finite; a program needn't handle non-finite values.
Results may differ from the reference program's by a relative error of at most 0.035.
Values may be sent and summed in bfloat16 or wider, within the bound.
No kernel may reach another device: no remote copies, remote signals or barrier semaphores. Data moves between devices by JAX's collectives and lax.ppermute only.
A program may use at most 192 MiB of HBM per device.

```python
import jax
import jax.numpy as jnp
from jax import lax

D = 768
HEADS = 12
HEAD_DIM = 64
FF = 3072
SEG = 128
NBLK = 8
LENGTH = 1024
NSEQ = 16


def levels(key, shape, shards, low, top_value):
    def one(dim, blocks):
        steps = jax.random.uniform(jax.random.fold_in(jax.random.fold_in(key, 6), dim), (blocks,), jnp.float32, low / len(shards), top_value / len(shards))
        return jnp.repeat(jnp.exp(steps), shape[dim] // blocks).reshape((-1,) + (1,) * (len(shape) - dim - 1))

    level = one(*shards[0])
    for cut in shards[1:]:
        level = level * one(*cut)
    return level


def scatter_about(rng, shape, scale, reach, cuts=(), held_as=jnp.bfloat16):
    drawn = scale * jax.random.normal(rng, shape, jnp.float32)
    if cuts:
        drawn = drawn * levels(rng, shape, cuts, -0.22, 0.18)
    return jnp.clip(drawn, -reach, reach).astype(held_as)


def setup_inputs(seed: int = 0) -> dict:
    streams_of = jax.random.split(jax.random.key(seed), 17)
    return {
        "layer_input": scatter_about(streams_of[0], (NSEQ, LENGTH, D), 1.0, 6.0, ((0, 4), (1, 8))),
        "block_order": jax.vmap(lambda own: jax.random.permutation(own, NBLK))(jax.random.split(streams_of[1], NSEQ)).reshape((NSEQ, NBLK)).astype(jnp.int32),
        "attn_gain": jnp.clip(1.0 + 0.12 * jax.random.normal(streams_of[2], (D,), jnp.float32), 0.3984375, 1.59375).astype(jnp.bfloat16),
        "attn_shift": scatter_about(streams_of[3], (D,), 0.5, 3.0, ((0, 8),)),
        "w_qkv": scatter_about(streams_of[4], (D, 3 * D), D ** -0.5, 0.21875, ((0, 8),)),
        "bias_query": scatter_about(streams_of[5], (D,), 0.5, 3.0, ((0, 8),)),
        "bias_value": scatter_about(streams_of[6], (D,), 0.5, 3.0, ((0, 8),)),
        "w_out": scatter_about(streams_of[7], (D, D), 0.5, 3.0, ((0, 8),)),
        "bias_out": scatter_about(streams_of[8], (D,), 0.5, 3.0, ((0, 8),)),
        "mlp_gain": jnp.clip(1.0 + 0.12 * jax.random.normal(streams_of[9], (D,), jnp.float32), 0.3984375, 1.59375).astype(jnp.bfloat16),
        "mlp_shift": scatter_about(streams_of[10], (D,), 0.5, 3.0, ((0, 8),)),
        "w_up": scatter_about(streams_of[11], (D, FF), D ** -0.5, 0.21875, ((0, 8),)),
        "bias_up": scatter_about(streams_of[12], (FF,), 0.5, 3.0, ((0, 8),)),
        "w_down": scatter_about(streams_of[13], (FF, D), FF ** -0.5, 0.109375, ((0, 8),)),
        "bias_down": scatter_about(streams_of[14], (D,), 0.5, 3.0, ((0, 8),)),
        "cotangent": scatter_about(streams_of[15], (NSEQ, LENGTH, D), 1.0, 6.0, ((0, 4), (1, 8))),
    }


@jax.custom_vjp
def low(v):
    return lax.optimization_barrier(v.astype(jnp.bfloat16)).astype(jnp.float32)

@jax.custom_vjp
def low_back(v):
    return v

def low_keep(v):
    return (low(v), None)

def low_pass(kept, grad):
    return (grad,)

def back_keep(v):
    return (v, None)

def back_low(kept, grad):
    return (low(grad),)
low.defvjp(low_keep, low_pass)
low_back.defvjp(back_keep, back_low)

def matmul(left, right):
    return jnp.dot(left, right, precision=lax.Precision.HIGHEST, preferred_element_type=jnp.float32)

def layer_norm(values, gain_vec, shift_vec):
    row_mean = lax.optimization_barrier(jnp.mean(values, axis=-1, keepdims=True))
    centred = values - row_mean
    row_var = lax.optimization_barrier(jnp.mean(centred * centred, axis=-1, keepdims=True))
    return centred * lax.rsqrt(row_var + 1e-05) * gain_vec + shift_vec

def gelu_tanh(up_in):
    return 0.5 * up_in * (1.0 + jnp.tanh(0.7978845608028654 * (up_in + 0.044715 * up_in * up_in * up_in)))

def forward(seq_input, params, positions):
    attn_gain, attn_shift, w_qkv, bias_query, bias_value, w_out, bias_out, mlp_gain, mlp_shift, w_up, bias_up, w_down, bias_down = params
    length = seq_input.shape[0]
    model_width = seq_input.shape[1]
    normed = low(layer_norm(seq_input, attn_gain, attn_shift))
    qkv_bias = jnp.concatenate([bias_query, jnp.zeros_like(bias_query), bias_value])
    qkv = low_back(low(matmul(normed, w_qkv) + qkv_bias)).reshape(length, 3, HEADS, HEAD_DIM)
    queries = qkv[:, 0]
    key_rows = qkv[:, 1]
    value_rows = qkv[:, 2]
    scaling = HEAD_DIM ** (-0.5)
    block_size = min(512, length)

    def attend(block_args):
        query_block, query_pos = block_args
        scores = jnp.einsum('qhd,khd->hqk', query_block, key_rows, precision=lax.Precision.HIGHEST) * scaling
        scores = low_back(scores)
        visible = positions[None, None, :] <= query_pos[None, :, None]
        scores = jnp.where(visible, scores, -1e+30)
        top_score = lax.optimization_barrier(jnp.max(scores, axis=-1, keepdims=True))
        expo = jnp.exp(scores - top_score)
        probability = expo / lax.optimization_barrier(jnp.sum(expo, axis=-1, keepdims=True))
        return jnp.einsum('hqk,khd->qhd', low(probability), value_rows, precision=lax.Precision.HIGHEST)
    attended = lax.map(jax.checkpoint(attend), (queries.reshape(length // block_size, block_size, HEADS, HEAD_DIM), positions.reshape(length // block_size, block_size)))
    context = low_back(low(attended.reshape(length, model_width)))
    hidden = seq_input + low_back(matmul(context, w_out) + bias_out)
    normed_m = low(layer_norm(hidden, mlp_gain, mlp_shift))
    up_proj = low_back(matmul(normed_m, w_up) + bias_up)
    active = low(gelu_tanh(up_proj))
    return hidden + matmul(active, w_down) + bias_down

def reference(layer_input, block_order, attn_gain, attn_shift, w_qkv, bias_query, bias_value, w_out, bias_out, mlp_gain, mlp_shift, w_up, bias_up, w_down, bias_down, cotangent):
    params = (attn_gain.astype(jnp.float32), attn_shift.astype(jnp.float32), w_qkv.astype(jnp.float32), bias_query.astype(jnp.float32), bias_value.astype(jnp.float32), w_out.astype(jnp.float32), bias_out.astype(jnp.float32), mlp_gain.astype(jnp.float32), mlp_shift.astype(jnp.float32), w_up.astype(jnp.float32), bias_up.astype(jnp.float32), w_down.astype(jnp.float32), bias_down.astype(jnp.float32))

    def one_sequence(grad_total, seq_item):
        seq_input, order_row, seq_cotangent = seq_item
        positions = (jnp.repeat(order_row.astype(jnp.int32), SEG) * SEG + jnp.tile(jnp.arange(SEG, dtype=jnp.int32), NBLK)).astype(jnp.int32)
        output_seq, pullback = jax.vjp(lambda inner, weights: forward(inner, weights, positions), seq_input.astype(jnp.float32), params)
        grad_seq, grad_params = pullback(seq_cotangent.astype(jnp.float32))
        grad_total = jax.tree.map(jnp.add, grad_total, grad_params)
        return (grad_total, (output_seq.astype(jnp.bfloat16), grad_seq.astype(jnp.bfloat16)))
    zero_grads = jax.tree.map(jnp.zeros_like, params)
    totals, (layer_output, grad_input) = lax.scan(one_sequence, zero_grads, (layer_input, block_order, cotangent))
    return (layer_output, grad_input, totals[0], totals[1], totals[2], totals[3], totals[4], totals[5], totals[6], totals[7], totals[8], totals[9], totals[10], totals[11], totals[12])
```

```python
import jax
import jax.numpy as jnp
from jax import lax
from jax.sharding import PartitionSpec as P

HEAD_DIM = 64


NEG_BIG = -1e30


def layer_norm(values, gain_vec, shift_vec):
    row_mean = jnp.mean(values, axis=-1, keepdims=True)
    centred = values - row_mean
    row_var = jnp.mean(centred * centred, axis=-1, keepdims=True)
    return centred * lax.rsqrt(row_var + 1e-05) * gain_vec + shift_vec


def gelu_tanh(up_in):
    return (
        0.5
        * up_in
        * (1.0 + jnp.tanh(0.7978845608028654 * (up_in + 0.044715 * up_in * up_in * up_in)))
    )


def shard_count():
    return lax.axis_size("dp") * lax.axis_size("ctx")


def padded_length(length, multiple):
    return -(-length // multiple) * multiple


def gather_packed(pieces):
    count = shard_count()
    flat = [piece.reshape(-1) for piece in pieces]
    length = sum(item.size for item in flat)
    padded = padded_length(length, 1024)
    if padded > length:
        flat.append(jnp.zeros((padded - length,), flat[0].dtype))
    tiles = jnp.concatenate(flat).reshape(padded // 128, 128)
    full = lax.all_gather(tiles, ("dp", "ctx"), axis=0, tiled=True).reshape(count, padded)
    result = []
    offset = 0
    for piece in pieces:
        size = piece.size
        part = full[:, offset : offset + size].reshape((-1,) + piece.shape[1:])
        result.append(part)
        offset += size
    return result


def reduce_packed(grads):
    count = shard_count()
    seq_devices = lax.axis_size("seq")
    rows = [grad.astype(jnp.bfloat16).reshape(count, -1) for grad in grads]
    length = sum(row.shape[1] for row in rows)
    padded = padded_length(length, 1024 * seq_devices)
    if padded > length:
        rows.append(jnp.zeros((count, padded - length), jnp.bfloat16))
    packed = jnp.concatenate(rows, axis=1).reshape(count * padded // 128, 128)
    share = lax.psum_scatter(packed, ("dp", "ctx", "seq"), scatter_dimension=0, tiled=True)
    total = lax.all_gather(share, "seq", axis=0, tiled=True).reshape(-1)
    result = []
    offset = 0
    for grad in grads:
        size = grad.size // count
        shard_shape = (grad.shape[0] // count,) + grad.shape[1:]
        result.append(total[offset : offset + size].reshape(shard_shape).astype(jnp.float32))
        offset += size
    return result


def block_loop(row_count, step_fn, running):
    block_size = 512
    block_count = row_count // block_size
    return lax.fori_loop(
        0,
        block_count,
        lambda block_index, state_now: step_fn(state_now, block_index * block_size, block_size),
        running,
    )


def local(
    layer_input,
    block_order,
    attn_gain,
    attn_shift,
    w_qkv,
    bias_query,
    bias_value,
    w_out,
    bias_out,
    mlp_gain,
    mlp_shift,
    w_up,
    bias_up,
    w_down,
    bias_down,
    cotangent,
):
    f32 = jnp.float32
    bf16 = jnp.bfloat16
    shards = (
        attn_gain,
        attn_shift,
        w_qkv,
        bias_query,
        bias_value,
        w_out,
        bias_out,
        mlp_gain,
        mlp_shift,
        w_up,
        bias_up,
        w_down,
        bias_down,
    )
    gathered_a = gather_packed(shards[:9])
    gathered_m = gather_packed(shards[9:])
    whole = tuple(gathered_a) + tuple(gathered_m)
    (
        whole_attn_gain,
        whole_attn_shift,
        whole_w_qkv,
        whole_bias_query,
        whole_bias_value,
        whole_w_out,
        whole_bias_out,
        whole_mlp_gain,
        whole_mlp_shift,
        whole_w_up,
        whole_bias_up,
        whole_w_down,
        whole_bias_down,
    ) = whole
    seq_count, seg_len, model_width = layer_input.shape
    seq_devices = lax.axis_size("seq")
    head_width = model_width // seq_devices
    head_groups = head_width // HEAD_DIM
    ctx_span = seg_len * seq_devices
    scaling = HEAD_DIM ** (-0.5)
    all_pos = jnp.repeat(block_order, seg_len, axis=1) * seg_len + jnp.tile(
        jnp.arange(seg_len, dtype=jnp.int32), block_order.shape[1]
    )
    query_pos = lax.dynamic_slice_in_dim(all_pos, lax.axis_index("ctx") * ctx_span, ctx_span, 1)
    input_f32 = layer_input.astype(f32)
    normed_a, pull_attn = jax.vjp(
        layer_norm, input_f32, whole_attn_gain.astype(f32), whole_attn_shift.astype(f32)
    )
    normed_ab = normed_a.astype(bf16)
    qkv_bias = jnp.concatenate(
        [whole_bias_query, jnp.zeros_like(whole_bias_query), whole_bias_value]
    ).astype(f32)
    qkv_pre = jnp.dot(normed_ab, whole_w_qkv, preferred_element_type=f32) + qkv_bias
    qkv_tok = qkv_pre.astype(bf16).reshape(seq_count, seg_len, 3, model_width)
    qkv_heads = lax.all_to_all(qkv_tok, "seq", split_axis=3, concat_axis=1, tiled=True)
    head_shape = (seq_count, ctx_span, head_groups, HEAD_DIM)
    queries = qkv_heads[:, :, 0].reshape(head_shape)
    key_rows = qkv_heads[:, :, 1].reshape(head_shape)
    value_rows = qkv_heads[:, :, 2].reshape(head_shape)
    stat_shape = (seq_count, ctx_span, head_groups)
    start_state = (
        jnp.full(stat_shape, NEG_BIG, f32),
        jnp.zeros(stat_shape, f32),
        jnp.zeros(head_shape, f32),
    )
    key_piece = lax.all_gather(key_rows, "ctx", axis=1, tiled=True)
    value_piece = lax.all_gather(value_rows, "ctx", axis=1, tiled=True)

    def step_fn(state_now, offset, block_size):
        run_max, denominator, accumulated = state_now
        key_block = lax.dynamic_slice_in_dim(key_piece, offset, block_size, 1)
        value_block = lax.dynamic_slice_in_dim(value_piece, offset, block_size, 1)
        key_pos = lax.dynamic_slice_in_dim(all_pos, offset, block_size, 1)
        scores = (
            jnp.einsum("nqhd,nkhd->nqhk", queries, key_block, preferred_element_type=f32) * scaling
        )
        visible = key_pos[:, None, None, :] <= query_pos[:, :, None, None]
        new_max = jnp.maximum(run_max, jnp.max(jnp.where(visible, scores, NEG_BIG), axis=-1))
        correction = jnp.exp(run_max - new_max)
        weights_p = jnp.where(visible, jnp.exp(scores - new_max[..., None]), 0.0)
        denominator = denominator * correction + jnp.sum(weights_p, axis=-1)
        accumulated = accumulated * correction[..., None] + jnp.einsum(
            "nqhk,nkhd->nqhd", weights_p.astype(bf16), value_block, preferred_element_type=f32
        )
        return (new_max, denominator, accumulated)

    run_max, denominator, accumulated = block_loop(key_piece.shape[1], step_fn, start_state)
    log_sum = run_max + jnp.log(denominator)
    attn_out = accumulated / denominator[..., None]
    ctx_heads = attn_out.reshape(seq_count, ctx_span, head_width).astype(bf16)
    context = lax.all_to_all(ctx_heads, "seq", split_axis=1, concat_axis=2, tiled=True)
    hidden = (
        input_f32
        + jnp.dot(context, whole_w_out, preferred_element_type=f32)
        + whole_bias_out.astype(f32)
    )
    normed_m, pull_mlp = jax.vjp(
        layer_norm, hidden, whole_mlp_gain.astype(f32), whole_mlp_shift.astype(f32)
    )
    normed_mb = normed_m.astype(bf16)
    up_in = jnp.dot(normed_mb, whole_w_up, preferred_element_type=f32) + whole_bias_up.astype(f32)
    active, pull_gelu = jax.vjp(gelu_tanh, up_in)
    active_b = active.astype(bf16)
    layer_output = (
        hidden
        + jnp.dot(active_b, whole_w_down, preferred_element_type=f32)
        + whole_bias_down.astype(f32)
    ).astype(bf16)
    back_w_qkv = whole_w_qkv
    back_w_out = whole_w_out
    back_w_up = whole_w_up
    back_w_down = whole_w_down
    grad_w_down = jnp.einsum("nsf,nsd->fd", active_b, cotangent, preferred_element_type=f32)
    grad_bias_down = jnp.sum(cotangent, axis=(0, 1), dtype=f32)
    grad_active = jnp.einsum("nsd,fd->nsf", cotangent, back_w_down, preferred_element_type=f32)
    (grad_up_f,) = pull_gelu(grad_active)
    grad_up = grad_up_f.astype(bf16)
    grad_w_up = jnp.einsum("nsd,nsf->df", normed_mb, grad_up, preferred_element_type=f32)
    grad_bias_up = jnp.sum(grad_up, axis=(0, 1), dtype=f32)
    grad_normed_m = jnp.einsum("nsf,df->nsd", grad_up, back_w_up, preferred_element_type=f32)
    grad_hidden_norm, grad_mlp_gain, grad_mlp_shift = pull_mlp(grad_normed_m)
    grad_hidden = cotangent.astype(f32) + grad_hidden_norm
    grad_att = grad_hidden.astype(bf16)
    grad_w_out = jnp.einsum("nsc,nsd->cd", context, grad_att, preferred_element_type=f32)
    grad_bias_out = jnp.sum(grad_att, axis=(0, 1), dtype=f32)
    grad_context = jnp.einsum(
        "nsd,cd->nsc", grad_att, back_w_out, preferred_element_type=f32
    ).astype(bf16)
    grad_out_h = lax.all_to_all(
        grad_context, "seq", split_axis=2, concat_axis=1, tiled=True
    ).reshape(head_shape)
    delta = jnp.sum(grad_out_h.astype(f32) * attn_out, axis=-1)

    def query_grads(
        query_block, gradout_block, key_block, value_block, visible, lse_block, delta_block
    ):
        scores = (
            jnp.einsum("nqhd,nkhd->nqhk", query_block, key_block, preferred_element_type=f32)
            * scaling
        )
        probability = jnp.where(visible, jnp.exp(scores - lse_block[..., None]), 0.0)
        grad_prob = jnp.einsum(
            "nqhd,nkhd->nqhk", gradout_block, value_block, preferred_element_type=f32
        )
        grad_scores = (probability * (grad_prob - delta_block[..., None])).astype(bf16)
        return (probability, grad_scores)

    dq_key_piece = lax.all_gather(key_rows, "ctx", axis=1, tiled=True)
    dq_value_piece = lax.all_gather(value_rows, "ctx", axis=1, tiled=True)

    def step_fn(grad_query, offset, block_size):
        key_block = lax.dynamic_slice_in_dim(dq_key_piece, offset, block_size, 1)
        value_block = lax.dynamic_slice_in_dim(dq_value_piece, offset, block_size, 1)
        key_pos = lax.dynamic_slice_in_dim(all_pos, offset, block_size, 1)
        visible = key_pos[:, None, None, :] <= query_pos[:, :, None, None]
        probability, grad_scores = query_grads(
            queries, grad_out_h, key_block, value_block, visible, log_sum, delta
        )
        return (
            grad_query
            + jnp.einsum("nqhk,nkhd->nqhd", grad_scores, key_block, preferred_element_type=f32)
            * scaling
        )

    grad_query = block_loop(dq_key_piece.shape[1], step_fn, jnp.zeros(head_shape, f32))
    gathered_lse, gathered_delta = (
        lax.all_gather(log_sum.astype(jnp.bfloat16), "ctx", axis=1, tiled=True).astype(
            log_sum.dtype
        ),
        lax.all_gather(delta.astype(jnp.bfloat16), "ctx", axis=1, tiled=True).astype(delta.dtype),
    )
    query_piece = lax.all_gather(queries, "ctx", axis=1, tiled=True)
    gradout_piece = lax.all_gather(grad_out_h, "ctx", axis=1, tiled=True)

    def step_fn(state_now, offset, block_size):
        grad_key, grad_value = state_now
        query_block = lax.dynamic_slice_in_dim(query_piece, offset, block_size, 1)
        gradout_block = lax.dynamic_slice_in_dim(gradout_piece, offset, block_size, 1)
        block_pos = lax.dynamic_slice_in_dim(all_pos, offset, block_size, 1)
        lse_block = lax.dynamic_slice_in_dim(gathered_lse, offset, block_size, 1)
        delta_block = lax.dynamic_slice_in_dim(gathered_delta, offset, block_size, 1)
        visible = query_pos[:, None, None, :] <= block_pos[:, :, None, None]
        probability, grad_scores = query_grads(
            query_block, gradout_block, key_rows, value_rows, visible, lse_block, delta_block
        )
        grad_value = grad_value + jnp.einsum(
            "nqhk,nqhd->nkhd", probability.astype(bf16), gradout_block, preferred_element_type=f32
        )
        grad_key = (
            grad_key
            + jnp.einsum("nqhk,nqhd->nkhd", grad_scores, query_block, preferred_element_type=f32)
            * scaling
        )
        return (grad_key, grad_value)

    grad_key, grad_value = block_loop(
        query_piece.shape[1], step_fn, (jnp.zeros(head_shape, f32), jnp.zeros(head_shape, f32))
    )
    flat_shape = (seq_count, ctx_span, head_width)
    grad_qkv_heads = jnp.stack(
        [
            grad_query.astype(bf16).reshape(flat_shape),
            grad_key.astype(bf16).reshape(flat_shape),
            grad_value.astype(bf16).reshape(flat_shape),
        ],
        2,
    )
    grad_qkv = lax.all_to_all(
        grad_qkv_heads, "seq", split_axis=1, concat_axis=3, tiled=True
    ).reshape(seq_count, seg_len, 3 * model_width)
    grad_w_qkv = jnp.einsum("nsd,nsc->dc", normed_ab, grad_qkv, preferred_element_type=f32)
    grad_bias_query = jnp.sum(grad_qkv[:, :, :model_width], axis=(0, 1), dtype=f32)
    grad_bias_value = jnp.sum(grad_qkv[:, :, 2 * model_width :], axis=(0, 1), dtype=f32)
    grad_normed_a = jnp.einsum("nsc,dc->nsd", grad_qkv, back_w_qkv, preferred_element_type=f32)
    grad_input_norm, grad_attn_gain, grad_attn_shift = pull_attn(grad_normed_a)
    grad_input = (grad_hidden + grad_input_norm).astype(bf16)
    mlp_totals = reduce_packed(
        (
            grad_w_out,
            grad_bias_out,
            grad_mlp_gain,
            grad_mlp_shift,
            grad_w_up,
            grad_bias_up,
            grad_w_down,
            grad_bias_down,
        )
    )
    attn_totals = reduce_packed(
        (grad_attn_gain, grad_attn_shift, grad_w_qkv, grad_bias_query, grad_bias_value)
    )
    return (layer_output, grad_input) + tuple(attn_totals) + tuple(mlp_totals)


def solution(mesh):
    placed = (
        P("dp", ("ctx", "seq"), None),
        P("dp", None),
        P(("dp", "ctx")),
        P(("dp", "ctx")),
        P(("dp", "ctx"), None),
        P(("dp", "ctx")),
        P(("dp", "ctx")),
        P(("dp", "ctx"), None),
        P(("dp", "ctx")),
        P(("dp", "ctx")),
        P(("dp", "ctx")),
        P(("dp", "ctx"), None),
        P(("dp", "ctx")),
        P(("dp", "ctx"), None),
        P(("dp", "ctx")),
        P("dp", ("ctx", "seq"), None),
    )
    return jax.shard_map(
        local,
        mesh=mesh,
        in_specs=placed,
        out_specs=(
            P("dp", ("ctx", "seq"), None),
            P("dp", ("ctx", "seq"), None),
            P(("dp", "ctx")),
            P(("dp", "ctx")),
            P(("dp", "ctx"), None),
            P(("dp", "ctx")),
            P(("dp", "ctx")),
            P(("dp", "ctx"), None),
            P(("dp", "ctx")),
            P(("dp", "ctx")),
            P(("dp", "ctx")),
            P(("dp", "ctx"), None),
            P(("dp", "ctx")),
            P(("dp", "ctx"), None),
            P(("dp", "ctx")),
        ),
        check_vma=False,
    )
```

```python
import jax
import jax.numpy as jnp
from jax import lax
from jax.sharding import PartitionSpec as P

HEAD_DIM = 64


NEG_BIG = -1e30


def layer_norm(values, gain_vec, shift_vec):
    row_mean = jnp.mean(values, axis=-1, keepdims=True)
    centred = values - row_mean
    row_var = jnp.mean(centred * centred, axis=-1, keepdims=True)
    return centred * lax.rsqrt(row_var + 1e-05) * gain_vec + shift_vec


def gelu_tanh(up_in):
    return (
        0.5
        * up_in
        * (1.0 + jnp.tanh(0.7978845608028654 * (up_in + 0.044715 * up_in * up_in * up_in)))
    )


def shard_count():
    return lax.axis_size("dp") * lax.axis_size("ctx")


def padded_length(length, multiple):
    return -(-length // multiple) * multiple


def gather_packed(pieces):
    count = shard_count()
    flat = [piece.reshape(-1) for piece in pieces]
    length = sum(item.size for item in flat)
    padded = padded_length(length, 1024)
    if padded > length:
        flat.append(jnp.zeros((padded - length,), flat[0].dtype))
    tiles = jnp.concatenate(flat).reshape(padded // 128, 128)
    full = lax.all_gather(tiles, ("dp", "ctx"), axis=0, tiled=True).reshape(count, padded)
    result = []
    offset = 0
    for piece in pieces:
        size = piece.size
        part = full[:, offset : offset + size].reshape((-1,) + piece.shape[1:])
        result.append(part)
        offset += size
    return result


def reduce_packed(grads):
    count = shard_count()
    seq_devices = lax.axis_size("seq")
    rows = [grad.astype(jnp.bfloat16).reshape(count, -1) for grad in grads]
    length = sum(row.shape[1] for row in rows)
    padded = padded_length(length, 1024 * seq_devices)
    if padded > length:
        rows.append(jnp.zeros((count, padded - length), jnp.bfloat16))
    packed = jnp.concatenate(rows, axis=1).reshape(count * padded // 128, 128)
    share = lax.psum_scatter(packed, ("dp", "ctx", "seq"), scatter_dimension=0, tiled=True)
    total = lax.all_gather(share, "seq", axis=0, tiled=True).reshape(-1)
    result = []
    offset = 0
    for grad in grads:
        size = grad.size // count
        shard_shape = (grad.shape[0] // count,) + grad.shape[1:]
        result.append(total[offset : offset + size].reshape(shard_shape).astype(jnp.float32))
        offset += size
    return result


def reduce_matrix(grad):
    share = lax.psum_scatter(
        grad.astype(jnp.bfloat16), ("dp", "ctx", "seq"), scatter_dimension=0, tiled=True
    )
    return lax.all_gather(share, "seq", axis=0, tiled=True).astype(jnp.float32)


def block_loop(row_count, step_fn, running):
    block_size = 512
    block_count = row_count // block_size
    return lax.fori_loop(
        0,
        block_count,
        lambda block_index, state_now: step_fn(state_now, block_index * block_size, block_size),
        running,
    )


def local(
    layer_input,
    block_order,
    attn_gain,
    attn_shift,
    w_qkv,
    bias_query,
    bias_value,
    w_out,
    bias_out,
    mlp_gain,
    mlp_shift,
    w_up,
    bias_up,
    w_down,
    bias_down,
    cotangent,
):
    f32 = jnp.float32
    bf16 = jnp.bfloat16
    shards = (
        attn_gain,
        attn_shift,
        w_qkv,
        bias_query,
        bias_value,
        w_out,
        bias_out,
        mlp_gain,
        mlp_shift,
        w_up,
        bias_up,
        w_down,
        bias_down,
    )
    vector_ids = (0, 1, 3, 4, 6, 7, 8, 10, 12)
    vectors = gather_packed(tuple(shards[index] for index in vector_ids))
    whole = [None] * len(shards)
    for index, value in zip(vector_ids, vectors):
        whole[index] = value
    for index in (2, 5, 9, 11):
        whole[index] = lax.all_gather(shards[index], ("dp", "ctx"), axis=0, tiled=True)
    (
        whole_attn_gain,
        whole_attn_shift,
        whole_w_qkv,
        whole_bias_query,
        whole_bias_value,
        whole_w_out,
        whole_bias_out,
        whole_mlp_gain,
        whole_mlp_shift,
        whole_w_up,
        whole_bias_up,
        whole_w_down,
        whole_bias_down,
    ) = whole
    seq_count, seg_len, model_width = layer_input.shape
    seq_devices = lax.axis_size("seq")
    head_width = model_width // seq_devices
    head_groups = head_width // HEAD_DIM
    ctx_span = seg_len * seq_devices
    scaling = HEAD_DIM ** (-0.5)
    all_pos = jnp.repeat(block_order, seg_len, axis=1) * seg_len + jnp.tile(
        jnp.arange(seg_len, dtype=jnp.int32), block_order.shape[1]
    )
    query_pos = lax.dynamic_slice_in_dim(all_pos, lax.axis_index("ctx") * ctx_span, ctx_span, 1)
    input_f32 = layer_input.astype(f32)
    normed_a, pull_attn = jax.vjp(
        layer_norm, input_f32, whole_attn_gain.astype(f32), whole_attn_shift.astype(f32)
    )
    normed_ab = normed_a.astype(bf16)
    qkv_bias = jnp.concatenate(
        [whole_bias_query, jnp.zeros_like(whole_bias_query), whole_bias_value]
    ).astype(f32)
    qkv_pre = jnp.dot(normed_ab, whole_w_qkv, preferred_element_type=f32) + qkv_bias
    qkv_tok = qkv_pre.astype(bf16).reshape(seq_count, seg_len, 3, model_width)
    qkv_heads = lax.all_to_all(qkv_tok, "seq", split_axis=3, concat_axis=1, tiled=True)
    head_shape = (seq_count, ctx_span, head_groups, HEAD_DIM)
    queries = qkv_heads[:, :, 0].reshape(head_shape)
    key_rows = qkv_heads[:, :, 1].reshape(head_shape)
    value_rows = qkv_heads[:, :, 2].reshape(head_shape)
    stat_shape = (seq_count, ctx_span, head_groups)
    start_state = (
        jnp.full(stat_shape, NEG_BIG, f32),
        jnp.zeros(stat_shape, f32),
        jnp.zeros(head_shape, f32),
    )
    key_piece = lax.all_gather(key_rows, "ctx", axis=1, tiled=True)
    value_piece = lax.all_gather(value_rows, "ctx", axis=1, tiled=True)

    def step_fn(state_now, offset, block_size):
        run_max, denominator, accumulated = state_now
        key_block = lax.dynamic_slice_in_dim(key_piece, offset, block_size, 1)
        value_block = lax.dynamic_slice_in_dim(value_piece, offset, block_size, 1)
        key_pos = lax.dynamic_slice_in_dim(all_pos, offset, block_size, 1)
        scores = (
            jnp.einsum("nqhd,nkhd->nqhk", queries, key_block, preferred_element_type=f32) * scaling
        )
        visible = key_pos[:, None, None, :] <= query_pos[:, :, None, None]
        new_max = jnp.maximum(run_max, jnp.max(jnp.where(visible, scores, NEG_BIG), axis=-1))
        correction = jnp.exp(run_max - new_max)
        weights_p = jnp.where(visible, jnp.exp(scores - new_max[..., None]), 0.0)
        denominator = denominator * correction + jnp.sum(weights_p, axis=-1)
        accumulated = accumulated * correction[..., None] + jnp.einsum(
            "nqhk,nkhd->nqhd", weights_p.astype(bf16), value_block, preferred_element_type=f32
        )
        return (new_max, denominator, accumulated)

    run_max, denominator, accumulated = block_loop(key_piece.shape[1], step_fn, start_state)
    log_sum = run_max + jnp.log(denominator)
    attn_out = accumulated / denominator[..., None]
    ctx_heads = attn_out.reshape(seq_count, ctx_span, head_width).astype(bf16)
    context = lax.all_to_all(ctx_heads, "seq", split_axis=1, concat_axis=2, tiled=True)
    hidden = (
        input_f32
        + jnp.dot(context, whole_w_out, preferred_element_type=f32)
        + whole_bias_out.astype(f32)
    )
    normed_m, pull_mlp = jax.vjp(
        layer_norm, hidden, whole_mlp_gain.astype(f32), whole_mlp_shift.astype(f32)
    )
    normed_mb = normed_m.astype(bf16)
    up_in = jnp.dot(normed_mb, whole_w_up, preferred_element_type=f32) + whole_bias_up.astype(f32)
    active, pull_gelu = jax.vjp(gelu_tanh, up_in)
    active_b = active.astype(bf16)
    layer_output = (
        hidden
        + jnp.dot(active_b, whole_w_down, preferred_element_type=f32)
        + whole_bias_down.astype(f32)
    ).astype(bf16)
    back_w_qkv = whole_w_qkv
    back_w_out = whole_w_out
    back_w_up = whole_w_up
    back_w_down = whole_w_down
    grad_w_down = jnp.einsum("nsf,nsd->fd", active_b, cotangent, preferred_element_type=f32)
    grad_bias_down = jnp.sum(cotangent, axis=(0, 1), dtype=f32)
    grad_active = jnp.einsum("nsd,fd->nsf", cotangent, back_w_down, preferred_element_type=f32)
    (grad_up_f,) = pull_gelu(grad_active)
    grad_up = grad_up_f.astype(bf16)
    grad_w_up = jnp.einsum("nsd,nsf->df", normed_mb, grad_up, preferred_element_type=f32)
    grad_bias_up = jnp.sum(grad_up, axis=(0, 1), dtype=f32)
    grad_normed_m = jnp.einsum("nsf,df->nsd", grad_up, back_w_up, preferred_element_type=f32)
    grad_hidden_norm, grad_mlp_gain, grad_mlp_shift = pull_mlp(grad_normed_m)
    grad_hidden = cotangent.astype(f32) + grad_hidden_norm
    grad_att = grad_hidden.astype(bf16)
    grad_w_out = jnp.einsum("nsc,nsd->cd", context, grad_att, preferred_element_type=f32)
    grad_bias_out = jnp.sum(grad_att, axis=(0, 1), dtype=f32)
    grad_context = jnp.einsum(
        "nsd,cd->nsc", grad_att, back_w_out, preferred_element_type=f32
    ).astype(bf16)
    grad_w_down, grad_w_up, grad_w_out, grad_context = lax.optimization_barrier(
        (grad_w_down, grad_w_up, grad_w_out, grad_context)
    )
    mlp_totals = {
        11: reduce_matrix(grad_w_down),
        9: reduce_matrix(grad_w_up),
        5: reduce_matrix(grad_w_out),
    }
    grad_out_h = lax.all_to_all(
        grad_context, "seq", split_axis=2, concat_axis=1, tiled=True
    ).reshape(head_shape)
    delta = jnp.sum(grad_out_h.astype(f32) * attn_out, axis=-1)

    def query_grads(
        query_block, gradout_block, key_block, value_block, visible, lse_block, delta_block
    ):
        scores = (
            jnp.einsum("nqhd,nkhd->nqhk", query_block, key_block, preferred_element_type=f32)
            * scaling
        )
        probability = jnp.where(visible, jnp.exp(scores - lse_block[..., None]), 0.0)
        grad_prob = jnp.einsum(
            "nqhd,nkhd->nqhk", gradout_block, value_block, preferred_element_type=f32
        )
        grad_scores = (probability * (grad_prob - delta_block[..., None])).astype(bf16)
        return (probability, grad_scores)

    dq_key_piece = lax.all_gather(key_rows, "ctx", axis=1, tiled=True)
    dq_value_piece = lax.all_gather(value_rows, "ctx", axis=1, tiled=True)

    def step_fn(grad_query, offset, block_size):
        key_block = lax.dynamic_slice_in_dim(dq_key_piece, offset, block_size, 1)
        value_block = lax.dynamic_slice_in_dim(dq_value_piece, offset, block_size, 1)
        key_pos = lax.dynamic_slice_in_dim(all_pos, offset, block_size, 1)
        visible = key_pos[:, None, None, :] <= query_pos[:, :, None, None]
        probability, grad_scores = query_grads(
            queries, grad_out_h, key_block, value_block, visible, log_sum, delta
        )
        return (
            grad_query
            + jnp.einsum("nqhk,nkhd->nqhd", grad_scores, key_block, preferred_element_type=f32)
            * scaling
        )

    grad_query = block_loop(dq_key_piece.shape[1], step_fn, jnp.zeros(head_shape, f32))
    gathered_lse, gathered_delta = (
        lax.all_gather(log_sum.astype(jnp.bfloat16), "ctx", axis=1, tiled=True).astype(
            log_sum.dtype
        ),
        lax.all_gather(delta.astype(jnp.bfloat16), "ctx", axis=1, tiled=True).astype(delta.dtype),
    )
    query_piece = lax.all_gather(queries, "ctx", axis=1, tiled=True)
    gradout_piece = lax.all_gather(grad_out_h, "ctx", axis=1, tiled=True)

    def step_fn(state_now, offset, block_size):
        grad_key, grad_value = state_now
        query_block = lax.dynamic_slice_in_dim(query_piece, offset, block_size, 1)
        gradout_block = lax.dynamic_slice_in_dim(gradout_piece, offset, block_size, 1)
        block_pos = lax.dynamic_slice_in_dim(all_pos, offset, block_size, 1)
        lse_block = lax.dynamic_slice_in_dim(gathered_lse, offset, block_size, 1)
        delta_block = lax.dynamic_slice_in_dim(gathered_delta, offset, block_size, 1)
        visible = query_pos[:, None, None, :] <= block_pos[:, :, None, None]
        probability, grad_scores = query_grads(
            query_block, gradout_block, key_rows, value_rows, visible, lse_block, delta_block
        )
        grad_value = grad_value + jnp.einsum(
            "nqhk,nqhd->nkhd", probability.astype(bf16), gradout_block, preferred_element_type=f32
        )
        grad_key = (
            grad_key
            + jnp.einsum("nqhk,nqhd->nkhd", grad_scores, query_block, preferred_element_type=f32)
            * scaling
        )
        return (grad_key, grad_value)

    grad_key, grad_value = block_loop(
        query_piece.shape[1], step_fn, (jnp.zeros(head_shape, f32), jnp.zeros(head_shape, f32))
    )
    flat_shape = (seq_count, ctx_span, head_width)
    grad_qkv_heads = jnp.stack(
        [
            grad_query.astype(bf16).reshape(flat_shape),
            grad_key.astype(bf16).reshape(flat_shape),
            grad_value.astype(bf16).reshape(flat_shape),
        ],
        2,
    )
    grad_qkv = lax.all_to_all(
        grad_qkv_heads, "seq", split_axis=1, concat_axis=3, tiled=True
    ).reshape(seq_count, seg_len, 3 * model_width)
    grad_w_qkv = jnp.einsum("nsd,nsc->dc", normed_ab, grad_qkv, preferred_element_type=f32)
    grad_bias_query = jnp.sum(grad_qkv[:, :, :model_width], axis=(0, 1), dtype=f32)
    grad_bias_value = jnp.sum(grad_qkv[:, :, 2 * model_width :], axis=(0, 1), dtype=f32)
    grad_normed_a = jnp.einsum("nsc,dc->nsd", grad_qkv, back_w_qkv, preferred_element_type=f32)
    grad_input_norm, grad_attn_gain, grad_attn_shift = pull_attn(grad_normed_a)
    grad_input = (grad_hidden + grad_input_norm).astype(bf16)
    grads = [
        grad_attn_gain,
        grad_attn_shift,
        grad_w_qkv,
        grad_bias_query,
        grad_bias_value,
        grad_w_out,
        grad_bias_out,
        grad_mlp_gain,
        grad_mlp_shift,
        grad_w_up,
        grad_bias_up,
        grad_w_down,
        grad_bias_down,
    ]
    totals = [None] * len(grads)
    vector_totals = reduce_packed(tuple(grads[index] for index in vector_ids))
    for index, value in zip(vector_ids, vector_totals):
        totals[index] = value
    for index in (11, 9, 5):
        totals[index] = mlp_totals[index]
    totals[2] = reduce_matrix(grads[2])
    return (layer_output, grad_input) + tuple(totals)


def solution(mesh):
    placed = (
        P("dp", ("ctx", "seq"), None),
        P("dp", None),
        P(("dp", "ctx")),
        P(("dp", "ctx")),
        P(("dp", "ctx"), None),
        P(("dp", "ctx")),
        P(("dp", "ctx")),
        P(("dp", "ctx"), None),
        P(("dp", "ctx")),
        P(("dp", "ctx")),
        P(("dp", "ctx")),
        P(("dp", "ctx"), None),
        P(("dp", "ctx")),
        P(("dp", "ctx"), None),
        P(("dp", "ctx")),
        P("dp", ("ctx", "seq"), None),
    )
    return jax.shard_map(
        local,
        mesh=mesh,
        in_specs=placed,
        out_specs=(
            P("dp", ("ctx", "seq"), None),
            P("dp", ("ctx", "seq"), None),
            P(("dp", "ctx")),
            P(("dp", "ctx")),
            P(("dp", "ctx"), None),
            P(("dp", "ctx")),
            P(("dp", "ctx")),
            P(("dp", "ctx"), None),
            P(("dp", "ctx")),
            P(("dp", "ctx")),
            P(("dp", "ctx")),
            P(("dp", "ctx"), None),
            P(("dp", "ctx")),
            P(("dp", "ctx"), None),
            P(("dp", "ctx")),
        ),
        check_vma=False,
    )
```
